512 devices in a mesh: var: 16 (over x, z_lo), dp: 32 (over y, z_hi, core).
Axes of the slice: x: 4, y: 4, z: 16 (z_hi: 4, z_lo: 4; z = z_hi * 4 + z_lo), core: 2. Of those that a mesh axis runs over, the one named last changes fastest.
Arguments:
- fields: bfloat16 [32, 64, 32, 128], P('dp', 'var'), may hold values from -6 to 6
- kernels: bfloat16 [64, 16, 512], P('var'), may hold values from -1.5 to 1.5
- level_map: int32 [64], P('var'), may hold values 0 or 1
- norm_gain_vector: float32 [512], replicated, may hold values from 0.1 to 1.9
- w_in: bfloat16 [512, 2048], replicated, may hold values from -0.25 to 0.25
- w_out: bfloat16 [2048, 512], replicated, may hold values from -0.125 to 0.125
- cotangent: bfloat16 [32, 16, 256, 512], P('dp', None, 'var'), may hold values from -6 to 6
Outputs:
- block_out: bfloat16 [32, 16, 256, 512], P('dp', None, 'var')
- kernel_grad: float32 [64, 16, 512], P('var', None, 'dp')
The draws below stay inside these ranges and needn't reach their ends.
Inputs may be any that keep to these rules, and one draw needn't show every extreme that they name: variable-level v belongs to pressure level v // 4 and enters its aggregate where level_map[v] is 1.
All inputs are finite; a program needn't handle non-finite values. No bound on the sum of `level_map` on one device may be relied on, other than what follows from the above.
Results may differ from the reference program's by a relative error of at most 0.013.
Values may be sent and summed in bfloat16 or wider, within the bound.
No kernel may reach another device: no remote copies, remote signals or barrier semaphores. Data moves between devices by JAX's collectives and lax.ppermute only.
A program may use at most 64 MiB of HBM per device.

```python
import jax
import jax.numpy as jnp
from jax import lax

E = 512
F = 2048
PATCH = 4
VAR_DEV = 4
WP = 32
HP = 8
LEVELS = 16
VARS = 64
BATCH = 32
NTOK = 256


def with_ends(drawn, own_key, smallest, high):
    shape = drawn.shape
    place = [jax.random.randint(jax.random.fold_in(own_key, axis), (), 0, shape[axis]) for axis in range(len(shape))]
    drawn = drawn.at[tuple(place)].set(smallest)
    longest = shape.index(max(shape))
    place[longest] = (place[longest] + 1) % shape[longest]
    return drawn.at[tuple(place)].set(high)


def spiked(values, key, source, target, blocks, factor):
    owner, partner = [(jnp.arange(values.shape[dim]) // (values.shape[dim] // blocks)).reshape([-1 if axis == dim else 1 for axis in range(values.ndim)]) for dim in (source, target)]
    chosen = jax.random.permutation(key, blocks)[partner]
    strong = (owner == chosen) | (owner == (partner + blocks // 2) % blocks)
    return jnp.where(strong, factor * values, values)


def steps_of(own_key, extent, cuts, low, largest):
    gain, own = 1.0, jax.random.fold_in(own_key, 6)
    for axis_at, blocks in cuts:
        draws = jnp.exp(jax.random.uniform(jax.random.fold_in(own, axis_at), (blocks,), jnp.float32, low / len(cuts), largest / len(cuts)))
        gain = gain * jnp.repeat(draws, extent[axis_at] // blocks).reshape([-1 if axis == axis_at else 1 for axis in range(len(extent))])
    return gain


def noise(own_key, dims, deviation, reach, pieces=(), kind=jnp.bfloat16):
    loudness = steps_of(own_key, dims, pieces, -0.22, 0.18) if pieces else 1.0
    result = jax.random.normal(own_key, dims, jnp.float32) * deviation * loudness
    return jnp.minimum(jnp.maximum(result, -reach), reach).astype(kind)


def heavy_noise(key, shape, deviation, limit, cuts, heavy, kind=jnp.bfloat16):
    result = deviation * jax.random.normal(key, shape, jnp.float32)
    if cuts:
        result = result * steps_of(key, shape, cuts, -0.22, 0.18)
    return jnp.clip(spiked(result, jax.random.fold_in(key, 3), *heavy), -limit, limit).astype(kind)


def setup_inputs(seed: int = 0) -> dict:
    seeds = jax.random.split(jax.random.key(seed), 8)
    return {
        "fields": noise(seeds[0], (BATCH, VARS, PATCH * HP, PATCH * WP), 1.0, 6.0, ((0, 32), (1, 16))),
        "kernels": noise(seeds[1], (VARS, PATCH * PATCH, E), (PATCH * PATCH) ** -0.5, 1.5, ((0, 16),)),
        "level_map": with_ends((jax.random.randint(seeds[2], (VARS,), 0, 2) < 1).astype(jnp.int32), jax.random.fold_in(seeds[2], 1), 0, 1),
        "norm_gain_vector": jnp.clip(1.0 + 0.18 * jax.random.normal(seeds[3], (E,), jnp.float32), 0.1, 1.9),
        "w_in": noise(seeds[4], (E, F), E ** -0.5, 0.25),
        "w_out": noise(seeds[5], (F, E), F ** -0.5, 0.125),
        "cotangent": heavy_noise(seeds[6], (BATCH, LEVELS, NTOK, E), 1.0, 6.0, ((0, 32), (2, 16)), (0, 3, 32, 2.75)),
    }


def patches_of(image):
    count_v, height, width = image.shape
    shaped = image.reshape(count_v, height // PATCH, PATCH, width // PATCH, PATCH)
    return shaped.transpose(0, 1, 3, 2, 4).reshape(count_v, height // PATCH * (width // PATCH), PATCH * PATCH)

def block_pass(token_rows, grads, norm_gain_vector, w_in, w_out):
    width = token_rows.shape[-1]
    rows = token_rows.reshape(-1, width).astype(jnp.float32)
    mean_row = lax.optimization_barrier(jnp.mean(rows, axis=1, keepdims=True))
    centered_rows = rows - mean_row
    reciprocal_std = lax.rsqrt(lax.optimization_barrier(jnp.mean(centered_rows * centered_rows, axis=1, keepdims=True)) + 1e-05)
    normalized_input = centered_rows * reciprocal_std
    normalized_rows = (normalized_input * norm_gain_vector).astype(jnp.bfloat16)
    pre = jnp.dot(normalized_rows, w_in, preferred_element_type=jnp.float32)
    hidden = jax.nn.gelu(pre, approximate=True).astype(jnp.bfloat16)
    output = (rows + jnp.dot(hidden, w_out, preferred_element_type=jnp.float32)).astype(jnp.bfloat16)
    gradient_rows = grads.reshape(-1, width)
    dhid = jnp.dot(gradient_rows, w_out.T, preferred_element_type=jnp.float32)
    gelu_back = jax.vjp(lambda value: jax.nn.gelu(value, approximate=True), pre)[1]
    dpre = gelu_back(dhid)[0].astype(jnp.bfloat16)
    dnorm = jnp.dot(dpre, w_in.T, preferred_element_type=jnp.float32)
    normalized_gradient = dnorm * norm_gain_vector
    token_gradient = gradient_rows.astype(jnp.float32) + reciprocal_std * (normalized_gradient - lax.optimization_barrier(jnp.mean(normalized_gradient, axis=1, keepdims=True)) - normalized_input * lax.optimization_barrier(jnp.mean(normalized_gradient * normalized_input, axis=1, keepdims=True)))
    return (output.reshape(token_rows.shape), token_gradient.astype(jnp.bfloat16).reshape(token_rows.shape))

def reference(fields, kernels, level_map, norm_gain_vector, w_in, w_out, cotangent):
    count_v = kernels.shape[0]
    level = jnp.arange(count_v, dtype=jnp.int32) // VAR_DEV
    weight = level_map.astype(jnp.float32)
    onehot = (level[None, :] == jnp.arange(LEVELS, dtype=jnp.int32)[:, None]).astype(jnp.float32) * weight[None, :]
    inv = 1.0 / jnp.maximum(lax.optimization_barrier(jnp.sum(onehot, axis=1)), 1.0)
    level_assignment = onehot * inv[:, None]
    level_member = inv[level] * weight
    kernels_flattened = kernels.astype(jnp.float32)

    def one_sample(pair):
        image, grads = pair
        patch_inputs = patches_of(image).astype(jnp.float32)
        patch_embeddings = jnp.einsum('ofm,omt->oft', patch_inputs, kernels_flattened)
        token_rows = jnp.einsum('ab,byd->ayd', level_assignment, patch_embeddings).astype(jnp.bfloat16)
        output, token_gradient = block_pass(token_rows, grads, norm_gain_vector, w_in, w_out)
        variable_gradient = jnp.take(token_gradient, level, axis=0).astype(jnp.float32)
        part = jnp.einsum('cjb,cjz->cbz', patch_inputs, variable_gradient) * level_member[:, None, None]
        return (output, part)
    outputs, parts = lax.map(one_sample, (fields, cotangent))
    scale = float(BATCH * NTOK) ** (-0.5)
    return (outputs, lax.optimization_barrier(jnp.sum(parts, axis=0)) * scale)
```

```python
import jax
import jax.numpy as jnp
from jax import lax
from jax.sharding import PartitionSpec as P

PATCH = 4


def patches_of(images):
    batch, count_v, height, width = images.shape
    shaped = images.reshape(batch, count_v, height // PATCH, PATCH, width // PATCH, PATCH)
    return shaped.transpose(0, 1, 2, 4, 3, 5).reshape(
        batch, count_v, height // PATCH * (width // PATCH), PATCH * PATCH
    )


def block_pass(token_rows, grads, norm_gain_vector, w_in, w_out):
    width = token_rows.shape[-1]
    rows = token_rows.reshape(-1, width).astype(jnp.float32)
    mean_row = jnp.mean(rows, axis=1, keepdims=True)
    centered_rows = rows - mean_row
    reciprocal_std = lax.rsqrt(
        jnp.mean(centered_rows * centered_rows, axis=1, keepdims=True) + 1e-05
    )
    normalized_input = centered_rows * reciprocal_std
    normalized_rows = (normalized_input * norm_gain_vector).astype(jnp.bfloat16)
    pre = jnp.dot(normalized_rows, w_in, preferred_element_type=jnp.float32)
    hidden = jax.nn.gelu(pre, approximate=True).astype(jnp.bfloat16)
    output = (rows + jnp.dot(hidden, w_out, preferred_element_type=jnp.float32)).astype(
        jnp.bfloat16
    )
    gradient_rows = grads.reshape(-1, width)
    dhid = jnp.dot(gradient_rows, w_out.T, preferred_element_type=jnp.float32)
    gelu_back = jax.vjp(lambda value: jax.nn.gelu(value, approximate=True), pre)[1]
    dpre = gelu_back(dhid)[0].astype(jnp.bfloat16)
    dnorm = jnp.dot(dpre, w_in.T, preferred_element_type=jnp.float32)
    normalized_gradient = dnorm * norm_gain_vector
    token_gradient = gradient_rows.astype(jnp.float32) + reciprocal_std * (
        normalized_gradient
        - jnp.mean(normalized_gradient, axis=1, keepdims=True)
        - normalized_input * jnp.mean(normalized_gradient * normalized_input, axis=1, keepdims=True)
    )
    return (
        output.reshape(token_rows.shape),
        token_gradient.astype(jnp.bfloat16).reshape(token_rows.shape),
    )


def level_tables(level, weight, groups):
    onehot = (level[None, :] == jnp.arange(groups, dtype=jnp.int32)[:, None]).astype(
        jnp.float32
    ) * weight[None, :]
    inv = 1.0 / jnp.maximum(jnp.sum(onehot, axis=1), 1.0)
    return (onehot * inv[:, None], inv[level] * weight)


def local(fields, kernels, level_map, norm_gain_vector, w_in, w_out, cotangent):
    batch, var_local = (fields.shape[0], fields.shape[1])
    patch_inputs = patches_of(fields)
    tokens_all = patch_inputs.shape[2]
    scale = float(batch * lax.axis_size("dp") * tokens_all) ** (-0.5)
    own_level = jnp.zeros((var_local,), jnp.int32)
    own_assign, own_member = level_tables(own_level, level_map.astype(jnp.float32), 1)
    patch_embeddings = jnp.einsum(
        "bvnp,vpe->bvne", patch_inputs, kernels, preferred_element_type=jnp.float32
    )
    token_rows = jnp.einsum("lv,bvne->blne", own_assign, patch_embeddings).astype(jnp.bfloat16)
    row_tokens = lax.all_to_all(token_rows, "var", split_axis=2, concat_axis=1, tiled=True)
    block_out, token_gradient = block_pass(row_tokens, cotangent, norm_gain_vector, w_in, w_out)
    dlevel = lax.all_to_all(token_gradient, "var", split_axis=1, concat_axis=2, tiled=True)
    partial_grad = (
        jnp.einsum("bvnp,bne->vpe", patch_inputs, dlevel[:, 0], preferred_element_type=jnp.float32)
        * own_member[:, None, None]
    )
    parts = lax.axis_size("dp")
    var_n, patch_n, width = partial_grad.shape
    pieces = partial_grad.reshape(var_n, patch_n, parts, width // parts)
    gathered = lax.all_to_all(pieces, "dp", split_axis=2, concat_axis=2, tiled=True)
    kernel_grad = jnp.sum(gathered, axis=2) * scale
    return (block_out, kernel_grad)


def solution(mesh):
    placed = (
        P("dp", "var", None, None),
        P("var", None, None),
        P("var"),
        P(),
        P(),
        P(),
        P("dp", None, "var", None),
    )
    return jax.shard_map(
        local,
        mesh=mesh,
        in_specs=placed,
        out_specs=(P("dp", None, "var", None), P("var", None, "dp")),
        check_vma=False,
    )
```

```python
import jax
import jax.numpy as jnp
from jax import lax
from jax.sharding import PartitionSpec as P

PATCH = 4


def patches_of(images):
    batch, count_v, height, width = images.shape
    shaped = images.reshape(batch, count_v, height // PATCH, PATCH, width // PATCH, PATCH)
    return shaped.transpose(0, 1, 2, 4, 3, 5).reshape(
        batch, count_v, height // PATCH * (width // PATCH), PATCH * PATCH
    )


def block_pass(token_rows, grads, norm_gain_vector, w_in, w_out):
    width = token_rows.shape[-1]
    rows = token_rows.reshape(-1, width).astype(jnp.float32)
    mean_row = jnp.mean(rows, axis=1, keepdims=True)
    centered_rows = rows - mean_row
    reciprocal_std = lax.rsqrt(
        jnp.mean(centered_rows * centered_rows, axis=1, keepdims=True) + 1e-05
    )
    normalized_input = centered_rows * reciprocal_std
    normalized_rows = (normalized_input * norm_gain_vector).astype(jnp.bfloat16)
    pre = jnp.dot(normalized_rows, w_in, preferred_element_type=jnp.float32)
    hidden = jax.nn.gelu(pre, approximate=True).astype(jnp.bfloat16)
    output = (rows + jnp.dot(hidden, w_out, preferred_element_type=jnp.float32)).astype(
        jnp.bfloat16
    )
    gradient_rows = grads.reshape(-1, width)
    dhid = jnp.dot(gradient_rows, w_out.T, preferred_element_type=jnp.float32)
    gelu_back = jax.vjp(lambda value: jax.nn.gelu(value, approximate=True), pre)[1]
    dpre = gelu_back(dhid)[0].astype(jnp.bfloat16)
    dnorm = jnp.dot(dpre, w_in.T, preferred_element_type=jnp.float32)
    normalized_gradient = dnorm * norm_gain_vector
    token_gradient = gradient_rows.astype(jnp.float32) + reciprocal_std * (
        normalized_gradient
        - jnp.mean(normalized_gradient, axis=1, keepdims=True)
        - normalized_input * jnp.mean(normalized_gradient * normalized_input, axis=1, keepdims=True)
    )
    return (
        output.reshape(token_rows.shape),
        token_gradient.astype(jnp.bfloat16).reshape(token_rows.shape),
    )


def level_tables(level, weight, groups):
    onehot = (level[None, :] == jnp.arange(groups, dtype=jnp.int32)[:, None]).astype(
        jnp.float32
    ) * weight[None, :]
    inv = 1.0 / jnp.maximum(jnp.sum(onehot, axis=1), 1.0)
    return (onehot * inv[:, None], inv[level] * weight)


def patch_rows(fields):
    batch, count_v, height, width = fields.shape
    shaped = fields.reshape(batch, count_v, height // PATCH, PATCH, width // PATCH, PATCH)
    return shaped.transpose(0, 2, 4, 1, 3, 5).reshape(
        batch, height // PATCH * (width // PATCH), count_v * PATCH * PATCH
    )


def local(fields, kernels, level_map, norm_gain_vector, w_in, w_out, cotangent):
    var_local, patch_n, width = kernels.shape
    parts = lax.axis_size("dp")
    rows = patch_rows(fields)
    batch, tokens_all = rows.shape[0], rows.shape[1]
    scale = float(batch * parts * tokens_all) ** (-0.5)
    own_level = jnp.zeros((var_local,), jnp.int32)
    _, own_member = level_tables(own_level, level_map.astype(jnp.float32), 1)
    weighted = (kernels.astype(jnp.float32) * own_member[:, None, None]).reshape(-1, width)
    token_rows = jnp.einsum(
        "bnk,ke->bne",
        rows.astype(jnp.float32),
        weighted,
        precision=lax.Precision.HIGHEST,
        preferred_element_type=jnp.float32,
    ).astype(jnp.bfloat16)
    chunks = lax.axis_size("var")
    token_rows = token_rows.reshape(batch, chunks, tokens_all // chunks, width)
    row_tokens = lax.all_to_all(token_rows, "var", split_axis=1, concat_axis=1, tiled=True)
    block_out, token_gradient = block_pass(row_tokens, cotangent, norm_gain_vector, w_in, w_out)
    dlevel = lax.all_to_all(token_gradient, "var", split_axis=1, concat_axis=1, tiled=True)
    dlevel = dlevel.reshape(batch, tokens_all, width)
    partial_grad = jnp.einsum("bne,bnk->ek", dlevel, rows, preferred_element_type=jnp.float32)
    pieces = partial_grad.reshape(parts, width // parts, var_local * patch_n)
    gathered = lax.all_to_all(pieces, "dp", split_axis=0, concat_axis=0, tiled=True)
    summed = jnp.sum(gathered, axis=0).T.reshape(var_local, patch_n, width // parts)
    kernel_grad = summed * (own_member * scale)[:, None, None]
    return (block_out, kernel_grad)


def solution(mesh):
    placed = (
        P("dp", "var", None, None),
        P("var", None, None),
        P("var"),
        P(),
        P(),
        P(),
        P("dp", None, "var", None),
    )
    return jax.shard_map(
        local,
        mesh=mesh,
        in_specs=placed,
        out_specs=(P("dp", None, "var", None), P("var", None, "dp")),
        check_vma=False,
    )
```

```python
import jax
import jax.numpy as jnp
from jax import lax
from jax.sharding import PartitionSpec as P

PATCH = 4


def patches_of(images):
    batch, count_v, height, width = images.shape
    shaped = images.reshape(batch, count_v, height // PATCH, PATCH, width // PATCH, PATCH)
    return shaped.transpose(0, 1, 2, 4, 3, 5).reshape(
        batch, count_v, height // PATCH * (width // PATCH), PATCH * PATCH
    )


def block_pass(token_rows, grads, norm_gain_vector, w_in, w_out):
    width = token_rows.shape[-1]
    rows = token_rows.reshape(-1, width).astype(jnp.float32)
    mean_row = jnp.mean(rows, axis=1, keepdims=True)
    centered_rows = rows - mean_row
    reciprocal_std = lax.rsqrt(
        jnp.mean(centered_rows * centered_rows, axis=1, keepdims=True) + 1e-05
    )
    normalized_input = centered_rows * reciprocal_std
    normalized_rows = (normalized_input * norm_gain_vector).astype(jnp.bfloat16)
    pre = jnp.dot(normalized_rows, w_in, preferred_element_type=jnp.float32)
    hidden = jax.nn.gelu(pre, approximate=True).astype(jnp.bfloat16)
    output = (rows + jnp.dot(hidden, w_out, preferred_element_type=jnp.float32)).astype(
        jnp.bfloat16
    )
    gradient_rows = grads.reshape(-1, width)
    dhid = jnp.dot(gradient_rows, w_out.T, preferred_element_type=jnp.float32)
    gelu_back = jax.vjp(lambda value: jax.nn.gelu(value, approximate=True), pre)[1]
    dpre = gelu_back(dhid)[0].astype(jnp.bfloat16)
    dnorm = jnp.dot(dpre, w_in.T, preferred_element_type=jnp.float32)
    normalized_gradient = dnorm * norm_gain_vector
    token_gradient = gradient_rows.astype(jnp.float32) + reciprocal_std * (
        normalized_gradient
        - jnp.mean(normalized_gradient, axis=1, keepdims=True)
        - normalized_input * jnp.mean(normalized_gradient * normalized_input, axis=1, keepdims=True)
    )
    return (
        output.reshape(token_rows.shape),
        token_gradient.astype(jnp.bfloat16).reshape(token_rows.shape),
    )


def level_tables(level, weight, groups):
    onehot = (level[None, :] == jnp.arange(groups, dtype=jnp.int32)[:, None]).astype(
        jnp.float32
    ) * weight[None, :]
    inv = 1.0 / jnp.maximum(jnp.sum(onehot, axis=1), 1.0)
    return (onehot * inv[:, None], inv[level] * weight)


def patch_rows(fields):
    batch, count_v, height, width = fields.shape
    shaped = fields.reshape(batch, count_v, height // PATCH, PATCH, width // PATCH, PATCH)
    return shaped.transpose(0, 2, 4, 1, 3, 5).reshape(
        batch, height // PATCH * (width // PATCH), count_v * PATCH * PATCH
    )


def local(fields, kernels, level_map, norm_gain_vector, w_in, w_out, cotangent):
    var_local, patch_n, width = kernels.shape
    parts = lax.axis_size("dp")
    rows = patch_rows(fields)
    batch, tokens_all = rows.shape[0], rows.shape[1]
    scale = float(batch * parts * tokens_all) ** (-0.5)
    own_level = jnp.zeros((var_local,), jnp.int32)
    _, own_member = level_tables(own_level, level_map.astype(jnp.float32), 1)
    weighted = (kernels.astype(jnp.float32) * own_member[:, None, None]).reshape(-1, width)
    token_rows = jnp.einsum(
        "bnk,ke->bne",
        rows.astype(jnp.float32),
        weighted,
        precision=lax.Precision.HIGHEST,
        preferred_element_type=jnp.float32,
    ).astype(jnp.bfloat16)
    chunks = lax.axis_size("var")
    token_rows = token_rows.reshape(batch, chunks, tokens_all // chunks, width)
    row_tokens = lax.all_to_all(token_rows, "var", split_axis=1, concat_axis=1, tiled=True)
    block_out, token_gradient = block_pass(row_tokens, cotangent, norm_gain_vector, w_in, w_out)
    dlevel = lax.all_to_all(token_gradient, "var", split_axis=1, concat_axis=1, tiled=True)
    dlevel = dlevel.reshape(batch, tokens_all, width)
    partial_grad = jnp.einsum("bne,bnk->ek", dlevel, rows, preferred_element_type=jnp.float32)
    pieces = partial_grad.reshape(parts, width // parts, var_local * patch_n).astype(jnp.bfloat16)
    gathered = lax.all_to_all(pieces, "dp", split_axis=0, concat_axis=0, tiled=True)
    summed = jnp.sum(gathered.astype(jnp.float32), axis=0).T.reshape(var_local, patch_n, width // parts)
    kernel_grad = summed * (own_member * scale)[:, None, None]
    return (block_out, kernel_grad)


def solution(mesh):
    placed = (
        P("dp", "var", None, None),
        P("var", None, None),
        P("var"),
        P(),
        P(),
        P(),
        P("dp", None, "var", None),
    )
    return jax.shard_map(
        local,
        mesh=mesh,
        in_specs=placed,
        out_specs=(P("dp", None, "var", None), P("var", None, "dp")),
        check_vma=False,
    )
```

```python
import jax
import jax.numpy as jnp
from jax import lax
from jax.sharding import PartitionSpec as P

PATCH = 4


def patches_of(images):
    batch, count_v, height, width = images.shape
    shaped = images.reshape(batch, count_v, height // PATCH, PATCH, width // PATCH, PATCH)
    return shaped.transpose(0, 1, 2, 4, 3, 5).reshape(
        batch, count_v, height // PATCH * (width // PATCH), PATCH * PATCH
    )


def block_pass(token_rows, grads, norm_gain_vector, w_in, w_out):
    width = token_rows.shape[-1]
    rows = token_rows.reshape(-1, width).astype(jnp.float32)
    mean_row = jnp.mean(rows, axis=1, keepdims=True)
    centered_rows = rows - mean_row
    reciprocal_std = lax.rsqrt(
        jnp.mean(centered_rows * centered_rows, axis=1, keepdims=True) + 1e-05
    )
    normalized_input = centered_rows * reciprocal_std
    normalized_rows = (normalized_input * norm_gain_vector).astype(jnp.bfloat16)
    pre = jnp.dot(normalized_rows, w_in, preferred_element_type=jnp.float32)
    hidden = jax.nn.gelu(pre, approximate=True).astype(jnp.bfloat16)
    output = (rows + jnp.dot(hidden, w_out, preferred_element_type=jnp.float32)).astype(
        jnp.bfloat16
    )
    gradient_rows = grads.reshape(-1, width)
    dhid = lax.optimization_barrier(jnp.dot(gradient_rows, w_out.T, preferred_element_type=jnp.float32))
    gelu_back = jax.vjp(lambda value: jax.nn.gelu(value, approximate=True), pre)[1]
    dpre = gelu_back(dhid)[0].astype(jnp.bfloat16)
    dnorm = jnp.dot(dpre, w_in.T, preferred_element_type=jnp.float32)
    normalized_gradient = dnorm * norm_gain_vector
    token_gradient = gradient_rows.astype(jnp.float32) + reciprocal_std * (
        normalized_gradient
        - jnp.mean(normalized_gradient, axis=1, keepdims=True)
        - normalized_input * jnp.mean(normalized_gradient * normalized_input, axis=1, keepdims=True)
    )
    return (
        output.reshape(token_rows.shape),
        token_gradient.astype(jnp.bfloat16).reshape(token_rows.shape),
    )


def level_tables(level, weight, groups):
    onehot = (level[None, :] == jnp.arange(groups, dtype=jnp.int32)[:, None]).astype(
        jnp.float32
    ) * weight[None, :]
    inv = 1.0 / jnp.maximum(jnp.sum(onehot, axis=1), 1.0)
    return (onehot * inv[:, None], inv[level] * weight)


def patch_rows(fields):
    batch, count_v, height, width = fields.shape
    shaped = fields.reshape(batch, count_v, height // PATCH, PATCH, width // PATCH, PATCH)
    return shaped.transpose(0, 2, 4, 1, 3, 5).reshape(
        batch, height // PATCH * (width // PATCH), count_v * PATCH * PATCH
    )


def local(fields, kernels, level_map, norm_gain_vector, w_in, w_out, cotangent):
    var_local, patch_n, width = kernels.shape
    parts = lax.axis_size("dp")
    rows = patch_rows(fields)
    batch, tokens_all = rows.shape[0], rows.shape[1]
    scale = float(batch * parts * tokens_all) ** (-0.5)
    own_level = jnp.zeros((var_local,), jnp.int32)
    _, own_member = level_tables(own_level, level_map.astype(jnp.float32), 1)
    weighted = (kernels.astype(jnp.float32) * own_member[:, None, None]).reshape(-1, width)
    token_rows = jnp.einsum(
        "bnk,ke->bne",
        rows.astype(jnp.float32),
        weighted,
        precision=lax.Precision.HIGHEST,
        preferred_element_type=jnp.float32,
    ).astype(jnp.bfloat16)
    chunks = lax.axis_size("var")
    token_rows = token_rows.reshape(batch, chunks, tokens_all // chunks, width)
    row_tokens = lax.all_to_all(token_rows, "var", split_axis=1, concat_axis=1, tiled=True)
    block_out, token_gradient = block_pass(row_tokens, cotangent, norm_gain_vector, w_in, w_out)
    dlevel = lax.all_to_all(token_gradient, "var", split_axis=1, concat_axis=1, tiled=True)
    dlevel = dlevel.reshape(batch, tokens_all, width)
    partial_grad = jnp.einsum("bne,bnk->ek", dlevel, rows, preferred_element_type=jnp.float32)
    pieces = partial_grad.reshape(parts, width // parts, var_local * patch_n).astype(jnp.bfloat16)
    gathered = lax.all_to_all(pieces, "dp", split_axis=0, concat_axis=0, tiled=True)
    summed = jnp.sum(gathered.astype(jnp.float32), axis=0).T.reshape(var_local, patch_n, width // parts)
    kernel_grad = summed * (own_member * scale)[:, None, None]
    return (block_out, kernel_grad)


def solution(mesh):
    placed = (
        P("dp", "var", None, None),
        P("var", None, None),
        P("var"),
        P(),
        P(),
        P(),
        P("dp", None, "var", None),
    )
    return jax.shard_map(
        local,
        mesh=mesh,
        in_specs=placed,
        out_specs=(P("dp", None, "var", None), P("var", None, "dp")),
        check_vma=False,
    )
```

```python
import jax
import jax.numpy as jnp
from jax import lax
from jax.sharding import PartitionSpec as P

PATCH = 4


def patches_of(images):
    batch, count_v, height, width = images.shape
    shaped = images.reshape(batch, count_v, height // PATCH, PATCH, width // PATCH, PATCH)
    return shaped.transpose(0, 1, 2, 4, 3, 5).reshape(
        batch, count_v, height // PATCH * (width // PATCH), PATCH * PATCH
    )


def block_pass(token_rows, grads, norm_gain_vector, w_in, w_out):
    width = token_rows.shape[-1]
    rows = token_rows.reshape(-1, width).astype(jnp.float32)
    mean_row = jnp.mean(rows, axis=1, keepdims=True)
    centered_rows = rows - mean_row
    reciprocal_std = lax.rsqrt(
        jnp.mean(centered_rows * centered_rows, axis=1, keepdims=True) + 1e-05
    )
    normalized_input = centered_rows * reciprocal_std
    normalized_rows = (normalized_input * norm_gain_vector).astype(jnp.bfloat16)
    pre = jnp.dot(normalized_rows, w_in, preferred_element_type=jnp.float32)
    hidden = jax.nn.gelu(pre, approximate=True).astype(jnp.bfloat16)
    output = (rows + jnp.dot(hidden, w_out, preferred_element_type=jnp.float32)).astype(
        jnp.bfloat16
    )
    gradient_rows = grads.reshape(-1, width)
    dhid = lax.optimization_barrier(jnp.dot(gradient_rows, w_out.T, preferred_element_type=jnp.float32))
    gelu_back = jax.vjp(lambda value: jax.nn.gelu(value, approximate=True), pre)[1]
    dpre = gelu_back(dhid)[0].astype(jnp.bfloat16)
    dnorm = jnp.dot(dpre, w_in.T, preferred_element_type=jnp.float32)
    normalized_gradient = dnorm * norm_gain_vector
    token_gradient = gradient_rows.astype(jnp.float32) + reciprocal_std * (
        normalized_gradient
        - jnp.mean(normalized_gradient, axis=1, keepdims=True)
        - normalized_input * jnp.mean(normalized_gradient * normalized_input, axis=1, keepdims=True)
    )
    return (
        output.reshape(token_rows.shape),
        token_gradient.astype(jnp.bfloat16).reshape(token_rows.shape),
    )


def level_tables(level, weight, groups):
    onehot = (level[None, :] == jnp.arange(groups, dtype=jnp.int32)[:, None]).astype(
        jnp.float32
    ) * weight[None, :]
    inv = 1.0 / jnp.maximum(jnp.sum(onehot, axis=1), 1.0)
    return (onehot * inv[:, None], inv[level] * weight)


def patch_rows(fields):
    batch, count_v, height, width = fields.shape
    shaped = fields.reshape(batch, count_v, height // PATCH, PATCH, width)
    shaped = shaped.transpose(0, 2, 1, 3, 4).reshape(batch, height // PATCH, count_v * PATCH, width)
    flipped = jnp.swapaxes(shaped, -1, -2)
    return flipped.reshape(batch, height // PATCH * (width // PATCH), PATCH * count_v * PATCH)


def local(fields, kernels, level_map, norm_gain_vector, w_in, w_out, cotangent):
    var_local, patch_n, width = kernels.shape
    parts = lax.axis_size("dp")
    rows = patch_rows(fields)
    batch, tokens_all = rows.shape[0], rows.shape[1]
    scale = float(batch * parts * tokens_all) ** (-0.5)
    own_level = jnp.zeros((var_local,), jnp.int32)
    _, own_member = level_tables(own_level, level_map.astype(jnp.float32), 1)
    weighted = (kernels.astype(jnp.float32) * own_member[:, None, None]).reshape(var_local, PATCH, PATCH, width)
    weighted = weighted.transpose(2, 0, 1, 3).reshape(-1, width)
    token_rows = jnp.einsum(
        "bnk,ke->bne",
        rows.astype(jnp.float32),
        weighted,
        precision=lax.Precision.HIGHEST,
        preferred_element_type=jnp.float32,
    ).astype(jnp.bfloat16)
    chunks = lax.axis_size("var")
    token_rows = token_rows.reshape(batch, chunks, tokens_all // chunks, width)
    row_tokens = lax.all_to_all(token_rows, "var", split_axis=1, concat_axis=1, tiled=True)
    block_out, token_gradient = block_pass(row_tokens, cotangent, norm_gain_vector, w_in, w_out)
    dlevel = lax.all_to_all(token_gradient, "var", split_axis=1, concat_axis=1, tiled=True)
    dlevel = dlevel.reshape(batch, tokens_all, width)
    partial_grad = jnp.einsum("bne,bnk->ek", dlevel, rows, preferred_element_type=jnp.float32)
    pieces = partial_grad.reshape(parts, width // parts, var_local * patch_n).astype(jnp.bfloat16)
    gathered = lax.all_to_all(pieces, "dp", split_axis=0, concat_axis=0, tiled=True)
    summed = jnp.sum(gathered.astype(jnp.float32), axis=0).T.reshape(PATCH, var_local, PATCH, width // parts)
    summed = summed.transpose(1, 2, 0, 3).reshape(var_local, patch_n, width // parts)
    kernel_grad = summed * (own_member * scale)[:, None, None]
    return (block_out, kernel_grad)


def solution(mesh):
    placed = (
        P("dp", "var", None, None),
        P("var", None, None),
        P("var"),
        P(),
        P(),
        P(),
        P("dp", None, "var", None),
    )
    return jax.shard_map(
        local,
        mesh=mesh,
        in_specs=placed,
        out_specs=(P("dp", None, "var", None), P("var", None, "dp")),
        check_vma=False,
    )
```

```python
import jax
import jax.numpy as jnp
from jax import lax
from jax.sharding import PartitionSpec as P

PATCH = 4


def patches_of(images):
    batch, count_v, height, width = images.shape
    shaped = images.reshape(batch, count_v, height // PATCH, PATCH, width // PATCH, PATCH)
    return shaped.transpose(0, 1, 2, 4, 3, 5).reshape(
        batch, count_v, height // PATCH * (width // PATCH), PATCH * PATCH
    )


def block_pass(token_rows, grads, norm_gain_vector, w_in, w_out):
    width = token_rows.shape[-1]
    rows = token_rows.reshape(-1, width).astype(jnp.float32)
    mean_row = jnp.mean(rows, axis=1, keepdims=True)
    centered_rows = rows - mean_row
    reciprocal_std = lax.rsqrt(
        jnp.mean(centered_rows * centered_rows, axis=1, keepdims=True) + 1e-05
    )
    normalized_input = centered_rows * reciprocal_std
    normalized_rows = (normalized_input * norm_gain_vector).astype(jnp.bfloat16)
    pre = jnp.dot(normalized_rows, w_in, preferred_element_type=jnp.float32)
    hidden = jax.nn.gelu(pre, approximate=True).astype(jnp.bfloat16)
    output = (rows + jnp.dot(hidden, w_out, preferred_element_type=jnp.float32)).astype(
        jnp.bfloat16
    )
    gradient_rows = grads.reshape(-1, width)
    dhid = lax.optimization_barrier(jnp.dot(gradient_rows, w_out.T, preferred_element_type=jnp.float32))
    gelu_back = jax.vjp(lambda value: jax.nn.gelu(value, approximate=True), pre)[1]
    dpre = gelu_back(dhid)[0].astype(jnp.bfloat16)
    dnorm = jnp.dot(dpre, w_in.T, preferred_element_type=jnp.float32)
    normalized_gradient = dnorm * norm_gain_vector
    token_gradient = gradient_rows.astype(jnp.float32) + reciprocal_std * (
        normalized_gradient
        - jnp.mean(normalized_gradient, axis=1, keepdims=True)
        - normalized_input * jnp.mean(normalized_gradient * normalized_input, axis=1, keepdims=True)
    )
    return (
        output.reshape(token_rows.shape),
        token_gradient.astype(jnp.bfloat16).reshape(token_rows.shape),
    )


def level_tables(level, weight, groups):
    onehot = (level[None, :] == jnp.arange(groups, dtype=jnp.int32)[:, None]).astype(
        jnp.float32
    ) * weight[None, :]
    inv = 1.0 / jnp.maximum(jnp.sum(onehot, axis=1), 1.0)
    return (onehot * inv[:, None], inv[level] * weight)


def patch_rows(fields):
    batch, count_v, height, width = fields.shape
    shaped = fields.reshape(batch, count_v, height // PATCH, PATCH, width)
    shaped = shaped.transpose(0, 2, 1, 3, 4).reshape(batch, height // PATCH, count_v * PATCH, width)
    flipped = jnp.swapaxes(shaped, -1, -2)
    return flipped.reshape(batch, height // PATCH * (width // PATCH), PATCH * count_v * PATCH)


def local(fields, kernels, level_map, norm_gain_vector, w_in, w_out, cotangent):
    var_local, patch_n, width = kernels.shape
    parts = lax.axis_size("dp")
    rows = patch_rows(fields)
    batch, tokens_all = rows.shape[0], rows.shape[1]
    scale = float(batch * parts * tokens_all) ** (-0.5)
    own_level = jnp.zeros((var_local,), jnp.int32)
    _, own_member = level_tables(own_level, level_map.astype(jnp.float32), 1)
    weighted = (kernels.astype(jnp.float32) * own_member[:, None, None]).reshape(var_local, PATCH, PATCH, width)
    weighted = weighted.transpose(2, 0, 1, 3).reshape(-1, width)
    token_rows = jnp.einsum(
        "bnk,ke->bne",
        rows.astype(jnp.float32),
        weighted,
        precision=lax.Precision.HIGH,
        preferred_element_type=jnp.float32,
    ).astype(jnp.bfloat16)
    chunks = lax.axis_size("var")
    token_rows = token_rows.reshape(batch, chunks, tokens_all // chunks, width)
    row_tokens = lax.all_to_all(token_rows, "var", split_axis=1, concat_axis=1, tiled=True)
    block_out, token_gradient = block_pass(row_tokens, cotangent, norm_gain_vector, w_in, w_out)
    dlevel = lax.all_to_all(token_gradient, "var", split_axis=1, concat_axis=1, tiled=True)
    dlevel = dlevel.reshape(batch, tokens_all, width)
    partial_grad = jnp.einsum("bne,bnk->ek", dlevel, rows, preferred_element_type=jnp.float32)
    pieces = partial_grad.reshape(parts, width // parts, var_local * patch_n).astype(jnp.bfloat16)
    gathered = lax.all_to_all(pieces, "dp", split_axis=0, concat_axis=0, tiled=True)
    summed = jnp.sum(gathered.astype(jnp.float32), axis=0).T.reshape(PATCH, var_local, PATCH, width // parts)
    summed = summed.transpose(1, 2, 0, 3).reshape(var_local, patch_n, width // parts)
    kernel_grad = summed * (own_member * scale)[:, None, None]
    return (block_out, kernel_grad)


def solution(mesh):
    placed = (
        P("dp", "var", None, None),
        P("var", None, None),
        P("var"),
        P(),
        P(),
        P(),
        P("dp", None, "var", None),
    )
    return jax.shard_map(
        local,
        mesh=mesh,
        in_specs=placed,
        out_specs=(P("dp", None, "var", None), P("var", None, "dp")),
        check_vma=False,
    )
```

```python
import jax
import jax.numpy as jnp
from jax import lax
from jax.sharding import PartitionSpec as P

PATCH = 4


def patches_of(images):
    batch, count_v, height, width = images.shape
    shaped = images.reshape(batch, count_v, height // PATCH, PATCH, width // PATCH, PATCH)
    return shaped.transpose(0, 1, 2, 4, 3, 5).reshape(
        batch, count_v, height // PATCH * (width // PATCH), PATCH * PATCH
    )


def block_pass(token_rows, grads, norm_gain_vector, w_in, w_out):
    width = token_rows.shape[-1]
    rows = token_rows.reshape(-1, width).astype(jnp.float32)
    mean_row = jnp.mean(rows, axis=1, keepdims=True)
    centered_rows = rows - mean_row
    reciprocal_std = lax.rsqrt(
        jnp.mean(centered_rows * centered_rows, axis=1, keepdims=True) + 1e-05
    )
    normalized_input = centered_rows * reciprocal_std
    normalized_rows = (normalized_input * norm_gain_vector).astype(jnp.bfloat16)
    pre = jnp.dot(normalized_rows, w_in, preferred_element_type=jnp.float32)
    hidden = jax.nn.gelu(pre, approximate=True).astype(jnp.bfloat16)
    output = (rows + jnp.dot(hidden, w_out, preferred_element_type=jnp.float32)).astype(
        jnp.bfloat16
    )
    gradient_rows = grads.reshape(-1, width)
    dhid = lax.optimization_barrier(jnp.dot(gradient_rows, w_out.T, preferred_element_type=jnp.float32).astype(jnp.bfloat16)).astype(jnp.float32)
    gelu_back = jax.vjp(lambda value: jax.nn.gelu(value, approximate=True), pre)[1]
    dpre = gelu_back(dhid)[0].astype(jnp.bfloat16)
    dnorm = jnp.dot(dpre, w_in.T, preferred_element_type=jnp.float32)
    normalized_gradient = dnorm * norm_gain_vector
    token_gradient = gradient_rows.astype(jnp.float32) + reciprocal_std * (
        normalized_gradient
        - jnp.mean(normalized_gradient, axis=1, keepdims=True)
        - normalized_input * jnp.mean(normalized_gradient * normalized_input, axis=1, keepdims=True)
    )
    return (
        output.reshape(token_rows.shape),
        token_gradient.astype(jnp.bfloat16).reshape(token_rows.shape),
    )


def level_tables(level, weight, groups):
    onehot = (level[None, :] == jnp.arange(groups, dtype=jnp.int32)[:, None]).astype(
        jnp.float32
    ) * weight[None, :]
    inv = 1.0 / jnp.maximum(jnp.sum(onehot, axis=1), 1.0)
    return (onehot * inv[:, None], inv[level] * weight)


def patch_rows(fields):
    batch, count_v, height, width = fields.shape
    shaped = fields.reshape(batch, count_v, height // PATCH, PATCH, width)
    shaped = shaped.transpose(0, 2, 1, 3, 4).reshape(batch, height // PATCH, count_v * PATCH, width)
    flipped = jnp.swapaxes(shaped, -1, -2)
    return flipped.reshape(batch, height // PATCH * (width // PATCH), PATCH * count_v * PATCH)


def local(fields, kernels, level_map, norm_gain_vector, w_in, w_out, cotangent):
    var_local, patch_n, width = kernels.shape
    parts = lax.axis_size("dp")
    rows = patch_rows(fields)
    batch, tokens_all = rows.shape[0], rows.shape[1]
    scale = float(batch * parts * tokens_all) ** (-0.5)
    own_level = jnp.zeros((var_local,), jnp.int32)
    _, own_member = level_tables(own_level, level_map.astype(jnp.float32), 1)
    weighted = (kernels.astype(jnp.float32) * own_member[:, None, None]).reshape(var_local, PATCH, PATCH, width)
    weighted = weighted.transpose(2, 0, 1, 3).reshape(-1, width)
    token_rows = jnp.einsum(
        "bnk,ke->bne",
        rows.astype(jnp.float32),
        weighted,
        precision=lax.Precision.HIGH,
        preferred_element_type=jnp.float32,
    ).astype(jnp.bfloat16)
    chunks = lax.axis_size("var")
    token_rows = token_rows.reshape(batch, chunks, tokens_all // chunks, width)
    row_tokens = lax.all_to_all(token_rows, "var", split_axis=1, concat_axis=1, tiled=True)
    block_out, token_gradient = block_pass(row_tokens, cotangent, norm_gain_vector, w_in, w_out)
    dlevel = lax.all_to_all(token_gradient, "var", split_axis=1, concat_axis=1, tiled=True)
    dlevel = dlevel.reshape(batch, tokens_all, width)
    partial_grad = jnp.einsum("bne,bnk->ek", dlevel, rows, preferred_element_type=jnp.float32)
    pieces = partial_grad.reshape(parts, width // parts, var_local * patch_n).astype(jnp.bfloat16)
    gathered = lax.all_to_all(pieces, "dp", split_axis=0, concat_axis=0, tiled=True)
    summed = jnp.sum(gathered.astype(jnp.float32), axis=0).T.reshape(PATCH, var_local, PATCH, width // parts)
    summed = summed.transpose(1, 2, 0, 3).reshape(var_local, patch_n, width // parts)
    kernel_grad = summed * (own_member * scale)[:, None, None]
    return (block_out, kernel_grad)


def solution(mesh):
    placed = (
        P("dp", "var", None, None),
        P("var", None, None),
        P("var"),
        P(),
        P(),
        P(),
        P("dp", None, "var", None),
    )
    return jax.shard_map(
        local,
        mesh=mesh,
        in_specs=placed,
        out_specs=(P("dp", None, "var", None), P("var", None, "dp")),
        check_vma=False,
    )
```
